256 devices in a mesh: gx: 8 (over x, core), gy: 8 (over z), gz: 4 (over y).
Axes of the slice: x: 4, y: 4, z: 8, core: 2. Of those that a mesh axis runs over, the one named last changes fastest.
Arguments:
- flat_weight: float32 [6144, 128, 128], P(('gx', 'gy', 'gz')), may hold values from -6 to 6
- flat_first: float32 [6144, 128, 128], P(('gx', 'gy', 'gz')), may hold values from -3 to 3
- flat_second: float32 [6144, 128, 128], P(('gx', 'gy', 'gz')), may hold values from 0.01 to 1
- tile_map: int32 [6144], P(('gx', 'gy', 'gz')), may hold values from 0 to 6143, as said below
- tile_seeds: int32 [64, 96], P(('gx', 'gy'), 'gz'), may hold values from 0 to 16777215
- tokens: bfloat16 [3072, 12288], P(('gy', 'gx'), 'gz'), may hold values from -6 to 6
- grad_out: bfloat16 [3072, 8192], P('gy', ('gx', 'gz')), may hold values from -6 to 6
Outputs:
- outputs: bfloat16 [3072, 8192], P('gy', ('gx', 'gz'))
- input_grad: bfloat16 [3072, 12288], P(('gy', 'gx'), 'gz')
- weight_new: float32 [8192, 12288], P(('gx', 'gy'), 'gz')
- first_new: float32 [8192, 12288], P(('gx', 'gy'), 'gz')
- second_new: float32 [8192, 12288], P(('gx', 'gy'), 'gz')
The draws below stay inside these ranges and needn't reach their ends.
Inputs may be any that keep to these rules, and one draw needn't show every extreme that they name: `tile_map`: every tile of the slab is held by exactly one slot. Device rank r = ((a * 8) + b) * 4 + c holds slots r * 24 onward; it holds only tiles of the block owned by some device with the same b, where the owner of rows 128 * R onward and columns 128 * C onward has a = R // 8, b = (R) % 8, c = C // 24. One device holds at most 2 tiles of one owner, and exactly 2 of some owner.
All inputs are finite; a program needn't handle non-finite values.
Results may differ from the reference program's by a relative error of at most 0.013.
Values may be sent and summed in bfloat16 or wider, within the bound.
No kernel may reach another device: no remote copies, remote signals or barrier semaphores. Data moves between devices by JAX's collectives and lax.ppermute only.
A program may use at most 128 MiB of HBM per device.

```python
import math
import jax
import jax.numpy as jnp
from jax import lax

D = 12288
S = 8192
TILE = 128
TOK_BLK = 384
TOKENS = 3072
ROW_TILES = 1
COL_TILES = 24
TILES_OWN = 24
MOST = 2
N_GX = 8
N_GY = 8
N_GZ = 4


def draw_tile_map(key, part):
    group_size = N_GX * N_GZ
    across = D // TILE

    def one_plane(plane):
        plane_key = jax.random.fold_in(key, plane)
        key_list = jax.random.split(plane_key, 5)
        outer = jax.random.permutation(key_list[0], group_size)
        inner = jax.random.permutation(key_list[1], group_size)
        values = jax.random.permutation(key_list[2], group_size)
        ordinal = jnp.arange(TILES_OWN)
        spots = 2 * (ordinal // (MOST + 1)) + (ordinal % (MOST + 1) == MOST).astype(jnp.int32)
        shifts = values[spots]
        owner = outer[(inner[:, None] + shifts[None, :]) % group_size]
        owner_keys = jax.random.split(key_list[3], group_size)
        tile_orders = jax.vmap(lambda one_key: jax.random.permutation(one_key, TILES_OWN))(owner_keys)
        local_tile = tile_orders[owner, ordinal[None, :]]
        owner_gx = owner // N_GZ
        owner_gz = owner % N_GZ
        row_block = (owner_gx * N_GY + plane) * ROW_TILES + local_tile // COL_TILES
        col_block = owner_gz * COL_TILES + local_tile % COL_TILES
        tile_ids = row_block * across + col_block
        slot_keys = jax.random.split(key_list[4], group_size)
        slot_orders = jax.vmap(lambda one_key: jax.random.permutation(one_key, TILES_OWN))(slot_keys)
        return jnp.take_along_axis(tile_ids, slot_orders, axis=1)
    planes = jax.vmap(one_plane)(jnp.arange(N_GY))
    planes = planes.reshape(N_GY, N_GX, N_GZ, TILES_OWN).transpose(1, 0, 2, 3)
    return planes.reshape(-1).astype(jnp.int32)


def place_ends(drawn, stream_key, smallest, top_value):
    dims = drawn.shape
    index_at = [jax.random.randint(jax.random.fold_in(stream_key, axis), (), 0, dims[axis]) for axis in range(len(dims))]
    drawn = drawn.at[tuple(index_at)].set(smallest)
    longest = dims.index(max(dims))
    index_at[longest] = (index_at[longest] + 1) % dims[longest]
    return drawn.at[tuple(index_at)].set(top_value)


def level_of(own_key, extent, cuts, least, largest):
    factor_of, own = 1.0, jax.random.fold_in(own_key, 6)
    for dim, blocks in cuts:
        heights = jnp.exp(jax.random.uniform(jax.random.fold_in(own, dim), (blocks,), jnp.float32, least / len(cuts), largest / len(cuts)))
        factor_of = factor_of * jnp.repeat(heights, extent[dim] // blocks).reshape([-1 if axis == dim else 1 for axis in range(len(extent))])
    return factor_of


def scatter_about(stream_key, dims, scale, reach, pieces=(), kind=jnp.bfloat16):
    loudness = level_of(stream_key, dims, pieces, -0.22, 0.18) if pieces else 1.0
    array = jax.random.normal(stream_key, dims, jnp.float32) * scale * loudness
    return jnp.minimum(jnp.maximum(array, -reach), reach).astype(kind)


def setup_inputs(seed: int = 0) -> dict:
    splits = jax.random.split(jax.random.key(seed), 8)
    flat_weight = scatter_about(splits[0], (N_GX * N_GY * N_GZ * TILES_OWN, TILE, TILE), 1.0, 6.0, ((0, 256),), jnp.float32)
    flat_first = scatter_about(splits[1], (N_GX * N_GY * N_GZ * TILES_OWN, TILE, TILE), 0.5, 3.0, ((0, 256),), jnp.float32)
    flat_second = jnp.clip(jnp.exp(math.log(1.0) - 4.6051702 * jax.random.uniform(splits[2], (N_GX * N_GY * N_GZ * TILES_OWN, TILE, TILE), jnp.float32) ** level_of(splits[2], (N_GX * N_GY * N_GZ * TILES_OWN, TILE, TILE), ((0, 256),), -0.2, 0.2)), 0.01, 1.0)
    tile_map = draw_tile_map(jax.random.fold_in(splits[7], 71), 0)
    tile_seeds = place_ends(jax.random.randint(splits[4], (S // TILE, D // TILE), 0, 16777216), jax.random.fold_in(splits[4], 1), 0, 16777215).astype(jnp.int32)
    tokens = scatter_about(splits[5], (TOKENS, D), 1.0, 6.0, ((0, 64), (1, 4)))
    grad_out = scatter_about(splits[6], (TOKENS, S), 1.0, 6.0, ((0, 8), (1, 32)))
    return dict(flat_weight=flat_weight, flat_first=flat_first, flat_second=flat_second, tile_map=tile_map, tile_seeds=tile_seeds, tokens=tokens, grad_out=grad_out)


BETA_ONE = 0.9
BETA_TWO = 0.95
LEARN_RATE = 0.01
WEIGHT_DECAY = 0.1
EPSILON = 1e-08
BIAS_ONE = 0.9999734386011125
BIAS_TWO = 0.994079470779666
DITHER_SCALE = 0.25

def dither(seeds, position):
    mixing = seeds + position * 1640531527
    mixing = mixing ^ mixing >> 15 & 131071
    mixing = mixing * 739982445
    mixing = mixing ^ mixing >> 12 & 1048575
    mixing = mixing * 695872825
    mixing = mixing ^ mixing >> 15 & 131071
    return (mixing & 65535).astype(jnp.float32) / 65536.0 - 0.5

def assemble(flat, tile_map):
    tile_stack = jnp.zeros(flat.shape, flat.dtype).at[tile_map].set(flat)
    tile_grid = tile_stack.reshape(S // TILE, D // TILE, TILE, TILE)
    return tile_grid.transpose(0, 2, 1, 3).reshape(S, D)

def reference(flat_weight, flat_first, flat_second, tile_map, tile_seeds, tokens, grad_out):
    weight = assemble(flat_weight, tile_map)
    first_moment = assemble(flat_first, tile_map)
    second_moment = assemble(flat_second, tile_map)
    factor = 1.0 / math.sqrt(D)
    weight_low = weight.astype(jnp.bfloat16)
    outputs = (factor * jnp.dot(tokens, weight_low.T, preferred_element_type=jnp.float32)).astype(jnp.bfloat16)
    band_rows = S // N_GX
    input_grad = jnp.zeros((TOKENS, D), jnp.float32)
    for block_id in range(N_GX):
        partial_term = factor * jnp.dot(grad_out[:, block_id * band_rows:(block_id + 1) * band_rows], weight_low[block_id * band_rows:(block_id + 1) * band_rows], preferred_element_type=jnp.float32)
        input_grad = input_grad + lax.optimization_barrier(partial_term.astype(jnp.bfloat16)).astype(jnp.float32)
    gradient = jnp.zeros((S, D), jnp.float32)
    for block_id in range(N_GY):
        grad_band = grad_out[block_id * TOK_BLK:(block_id + 1) * TOK_BLK]
        token_band = tokens[block_id * TOK_BLK:(block_id + 1) * TOK_BLK]
        partial_term = factor * jnp.dot(grad_band.T, token_band, preferred_element_type=jnp.float32)
        gradient = gradient + lax.optimization_barrier(partial_term.astype(jnp.bfloat16)).astype(jnp.float32)
    first_new = BETA_ONE * first_moment + (1.0 - BETA_ONE) * gradient
    second_new = BETA_TWO * second_moment + (1.0 - BETA_TWO) * gradient * gradient
    direction = first_new / BIAS_ONE / (jnp.sqrt(second_new / BIAS_TWO) + EPSILON) + WEIGHT_DECAY * weight
    moved = weight - LEARN_RATE * direction
    row_ids = lax.broadcasted_iota(jnp.int32, (S, D), 0)
    col_ids = lax.broadcasted_iota(jnp.int32, (S, D), 1)
    seed_full = jnp.repeat(jnp.repeat(tile_seeds, TILE, axis=0), TILE, axis=1)
    noise = dither(seed_full, row_ids % TILE * TILE + col_ids % TILE)
    weight_new = moved + jnp.abs(moved) * DITHER_SCALE * noise
    return (outputs, input_grad.astype(jnp.bfloat16), weight_new, first_new, second_new)
```

```python
import math

import jax
import jax.numpy as jnp
from jax import lax
from jax.sharding import PartitionSpec as P

D = 12288


BETA_ONE = 0.9
BETA_TWO = 0.95
LEARN_RATE = 0.01
WEIGHT_DECAY = 0.1
EPSILON = 1e-08
BIAS_ONE = 0.9999734386011125
BIAS_TWO = 0.994079470779666
DITHER_SCALE = 0.25


def dither(seeds, position):
    mixing = seeds + position * 1640531527
    mixing = mixing ^ mixing >> 15 & 131071
    mixing = mixing * 739982445
    mixing = mixing ^ mixing >> 12 & 1048575
    mixing = mixing * 695872825
    mixing = mixing ^ mixing >> 15 & 131071
    return (mixing & 65535).astype(jnp.float32) / 65536.0 - 0.5


def body(flat_weight, flat_first, flat_second, tile_map, tile_seeds, tokens, grad_out):
    size_gx = lax.axis_size("gx")
    size_gy = lax.axis_size("gy")
    size_gz = lax.axis_size("gz")
    group_size = size_gx * size_gz
    tiles_own = flat_weight.shape[0]
    tile_side = flat_weight.shape[1]
    row_tiles = tile_seeds.shape[0]
    col_tiles = tile_seeds.shape[1]
    capacity = max(2, (2 * tiles_own + group_size - 1) // group_size - 1)
    total_slots = group_size * capacity
    across = col_tiles * size_gz
    row_block = tile_map // across
    col_block = tile_map % across
    target = row_block // row_tiles // size_gy * size_gz + col_block // col_tiles
    local_tile = row_block % row_tiles * col_tiles + col_block % col_tiles
    ordinal = jnp.arange(tiles_own, dtype=jnp.int32)
    same_owner = (target[:, None] == target[None, :]) & (ordinal[None, :] < ordinal[:, None])
    ranking = jnp.sum(same_owner.astype(jnp.int32), axis=1)
    position = target * capacity + ranking
    slot_ids = jnp.arange(total_slots, dtype=jnp.int32)
    matches = (position[None, :] == slot_ids[:, None]).astype(jnp.int32)
    source = jnp.sum(matches * ordinal[None, :], axis=1)
    filled = jnp.sum(matches, axis=1).astype(jnp.float32)[:, None, None]
    labels = jnp.sum(matches * (local_tile[None, :] + 1), axis=1)
    grid_shape = (group_size, capacity, tile_side, tile_side)
    send_weight = (jnp.take(flat_weight, source, axis=0) * filled).astype(jnp.bfloat16)
    got_labels = lax.all_to_all(
        labels.reshape(group_size, capacity), ("gx", "gz"), split_axis=0, concat_axis=0, tiled=True
    )
    got_weight = lax.all_to_all(
        send_weight.reshape(grid_shape), ("gx", "gz"), split_axis=0, concat_axis=0, tiled=True
    )
    token_band = lax.all_gather(tokens, "gx", axis=0, tiled=True)
    got_weight, token_band = lax.optimization_barrier((got_weight, token_band))
    got_weight = got_weight.astype(jnp.float32)
    got_labels = got_labels.reshape(total_slots)
    wanted = jnp.arange(1, tiles_own + 1, dtype=jnp.int32)
    hits = (got_labels[None, :] == wanted[:, None]).astype(jnp.int32)
    picked = jnp.sum(hits * slot_ids[None, :], axis=1)

    def place(received):
        flat_tiles = jnp.take(received.reshape(total_slots, tile_side, tile_side), picked, axis=0)
        tile_grid = flat_tiles.reshape(row_tiles, col_tiles, tile_side, tile_side)
        return tile_grid.transpose(0, 2, 1, 3).reshape(row_tiles * tile_side, col_tiles * tile_side)

    weight = place(got_weight)
    weight_low = weight.astype(jnp.bfloat16)
    weight_band = lax.all_gather(weight_low, "gy", axis=0, tiled=True)
    send_moments = jnp.stack(
        [jnp.take(flat_first, source, axis=0) * filled, jnp.take(flat_second, source, axis=0) * filled],
        axis=1,
    ).astype(jnp.bfloat16)
    send_moments, weight_band = lax.optimization_barrier((send_moments, weight_band))
    got_moments = lax.all_to_all(
        send_moments.reshape(group_size, capacity, 2, tile_side, tile_side),
        ("gx", "gz"),
        split_axis=0,
        concat_axis=0,
        tiled=True,
    ).astype(jnp.float32).reshape(total_slots, 2, tile_side, tile_side)
    first_moment = place(got_moments[:, 0])
    second_moment = place(got_moments[:, 1])
    factor = 1.0 / math.sqrt(D)
    partial_out = factor * jnp.dot(token_band, weight_band.T, preferred_element_type=jnp.float32)
    outputs = lax.psum_scatter(
        partial_out.astype(jnp.bfloat16), "gz", scatter_dimension=1, tiled=True
    )
    grad_band = lax.all_gather(grad_out.T, "gz", axis=0, tiled=True).T
    input_grad = lax.psum_scatter(
        (factor * jnp.dot(grad_band, weight_band, preferred_element_type=jnp.float32)).astype(
            jnp.bfloat16
        ),
        "gx",
        scatter_dimension=0,
        tiled=True,
    )
    gradient = lax.psum_scatter(
        (
            factor
            * lax.dot_general(
                grad_band, token_band, (((0,), (0,)), ((), ())), preferred_element_type=jnp.float32
            )
        ).astype(jnp.bfloat16),
        "gy",
        scatter_dimension=0,
        tiled=True,
    ).astype(jnp.float32)
    first_new = BETA_ONE * first_moment + (1.0 - BETA_ONE) * gradient
    second_new = BETA_TWO * second_moment + (1.0 - BETA_TWO) * gradient * gradient
    direction = (
        first_new / BIAS_ONE / (jnp.sqrt(second_new / BIAS_TWO) + EPSILON) + WEIGHT_DECAY * weight
    )
    moved = weight - LEARN_RATE * direction
    block_shape = weight.shape
    row_ids = lax.broadcasted_iota(jnp.int32, block_shape, 0)
    col_ids = lax.broadcasted_iota(jnp.int32, block_shape, 1)
    seed_full = jnp.repeat(jnp.repeat(tile_seeds, tile_side, axis=0), tile_side, axis=1)
    noise = dither(seed_full, row_ids % tile_side * tile_side + col_ids % tile_side)
    weight_new = moved + jnp.abs(moved) * DITHER_SCALE * noise
    return (outputs, input_grad, weight_new, first_new, second_new)


def solution(mesh):
    return jax.shard_map(
        body,
        mesh=mesh,
        in_specs=(
            P(("gx", "gy", "gz"), None, None),
            P(("gx", "gy", "gz"), None, None),
            P(("gx", "gy", "gz"), None, None),
            P(("gx", "gy", "gz")),
            P(("gx", "gy"), "gz"),
            P(("gy", "gx"), "gz"),
            P("gy", ("gx", "gz")),
        ),
        out_specs=(
            P("gy", ("gx", "gz")),
            P(("gy", "gx"), "gz"),
            P(("gx", "gy"), "gz"),
            P(("gx", "gy"), "gz"),
            P(("gx", "gy"), "gz"),
        ),
        check_vma=False,
    )
```

```python
import math

import jax
import jax.numpy as jnp
from jax import lax
from jax.sharding import PartitionSpec as P

D = 12288


BETA_ONE = 0.9
BETA_TWO = 0.95
LEARN_RATE = 0.01
WEIGHT_DECAY = 0.1
EPSILON = 1e-08
BIAS_ONE = 0.9999734386011125
BIAS_TWO = 0.994079470779666
DITHER_SCALE = 0.25


def dither(seeds, position):
    mixing = seeds + position * 1640531527
    mixing = mixing ^ mixing >> 15 & 131071
    mixing = mixing * 739982445
    mixing = mixing ^ mixing >> 12 & 1048575
    mixing = mixing * 695872825
    mixing = mixing ^ mixing >> 15 & 131071
    return (mixing & 65535).astype(jnp.float32) / 65536.0 - 0.5


def body(flat_weight, flat_first, flat_second, tile_map, tile_seeds, tokens, grad_out):
    size_gx = lax.axis_size("gx")
    size_gy = lax.axis_size("gy")
    size_gz = lax.axis_size("gz")
    group_size = size_gx * size_gz
    tiles_own = flat_weight.shape[0]
    tile_side = flat_weight.shape[1]
    row_tiles = tile_seeds.shape[0]
    col_tiles = tile_seeds.shape[1]
    capacity = max(2, (2 * tiles_own + group_size - 1) // group_size - 1)
    total_slots = group_size * capacity
    across = col_tiles * size_gz
    row_block = tile_map // across
    col_block = tile_map % across
    target = row_block // row_tiles // size_gy * size_gz + col_block // col_tiles
    local_tile = row_block % row_tiles * col_tiles + col_block % col_tiles
    ordinal = jnp.arange(tiles_own, dtype=jnp.int32)
    same_owner = (target[:, None] == target[None, :]) & (ordinal[None, :] < ordinal[:, None])
    ranking = jnp.sum(same_owner.astype(jnp.int32), axis=1)
    position = target * capacity + ranking
    slot_ids = jnp.arange(total_slots, dtype=jnp.int32)
    matches = (position[None, :] == slot_ids[:, None]).astype(jnp.int32)
    source = jnp.sum(matches * ordinal[None, :], axis=1)
    filled = jnp.sum(matches, axis=1).astype(jnp.float32)[:, None, None]
    labels = jnp.sum(matches * (local_tile[None, :] + 1), axis=1)
    grid_shape = (group_size, capacity, tile_side, tile_side)
    send_weight = (jnp.take(flat_weight, source, axis=0) * filled).astype(jnp.bfloat16)
    got_labels = lax.all_to_all(
        labels.reshape(group_size, capacity), ("gx", "gz"), split_axis=0, concat_axis=0, tiled=True
    )
    got_weight = lax.all_to_all(
        send_weight.reshape(grid_shape), ("gx", "gz"), split_axis=0, concat_axis=0, tiled=True
    )
    token_band = lax.all_gather(tokens, "gx", axis=0, tiled=True)
    got_weight, token_band = lax.optimization_barrier((got_weight, token_band))
    got_weight = got_weight.astype(jnp.float32)
    got_labels = got_labels.reshape(total_slots)
    wanted = jnp.arange(1, tiles_own + 1, dtype=jnp.int32)
    hits = (got_labels[None, :] == wanted[:, None]).astype(jnp.int32)
    picked = jnp.sum(hits * slot_ids[None, :], axis=1)

    def place(received):
        flat_tiles = jnp.take(received.reshape(total_slots, tile_side, tile_side), picked, axis=0)
        tile_grid = flat_tiles.reshape(row_tiles, col_tiles, tile_side, tile_side)
        return tile_grid.transpose(0, 2, 1, 3).reshape(row_tiles * tile_side, col_tiles * tile_side)

    weight = place(got_weight)
    weight_low = weight.astype(jnp.bfloat16)
    send_moments = jnp.stack(
        [jnp.take(flat_first, source, axis=0) * filled, jnp.take(flat_second, source, axis=0) * filled],
        axis=1,
    ).astype(jnp.bfloat16)
    send_moments, weight_low = lax.optimization_barrier((send_moments, weight_low))
    got_moments = lax.all_to_all(
        send_moments.reshape(group_size, capacity, 2, tile_side, tile_side),
        ("gx", "gz"),
        split_axis=0,
        concat_axis=0,
        tiled=True,
    )
    weight_band = lax.all_gather(weight_low, "gy", axis=0, tiled=True)
    got_moments, weight_band = lax.optimization_barrier((got_moments, weight_band))
    got_moments = got_moments.astype(jnp.float32).reshape(total_slots, 2, tile_side, tile_side)
    first_moment = place(got_moments[:, 0])
    second_moment = place(got_moments[:, 1])
    factor = 1.0 / math.sqrt(D)
    partial_out = factor * jnp.dot(token_band, weight_band.T, preferred_element_type=jnp.float32)
    outputs = lax.psum_scatter(
        partial_out.astype(jnp.bfloat16), "gz", scatter_dimension=1, tiled=True
    )
    grad_band = lax.all_gather(grad_out.T, "gz", axis=0, tiled=True).T
    input_grad = lax.psum_scatter(
        (factor * jnp.dot(grad_band, weight_band, preferred_element_type=jnp.float32)).astype(
            jnp.bfloat16
        ),
        "gx",
        scatter_dimension=0,
        tiled=True,
    )
    gradient = lax.psum_scatter(
        (
            factor
            * lax.dot_general(
                grad_band, token_band, (((0,), (0,)), ((), ())), preferred_element_type=jnp.float32
            )
        ).astype(jnp.bfloat16),
        "gy",
        scatter_dimension=0,
        tiled=True,
    ).astype(jnp.float32)
    first_new = BETA_ONE * first_moment + (1.0 - BETA_ONE) * gradient
    second_new = BETA_TWO * second_moment + (1.0 - BETA_TWO) * gradient * gradient
    direction = (
        first_new / BIAS_ONE / (jnp.sqrt(second_new / BIAS_TWO) + EPSILON) + WEIGHT_DECAY * weight
    )
    moved = weight - LEARN_RATE * direction
    block_shape = weight.shape
    row_ids = lax.broadcasted_iota(jnp.int32, block_shape, 0)
    col_ids = lax.broadcasted_iota(jnp.int32, block_shape, 1)
    seed_full = jnp.repeat(jnp.repeat(tile_seeds, tile_side, axis=0), tile_side, axis=1)
    noise = dither(seed_full, row_ids % tile_side * tile_side + col_ids % tile_side)
    weight_new = moved + jnp.abs(moved) * DITHER_SCALE * noise
    return (outputs, input_grad, weight_new, first_new, second_new)


def solution(mesh):
    return jax.shard_map(
        body,
        mesh=mesh,
        in_specs=(
            P(("gx", "gy", "gz"), None, None),
            P(("gx", "gy", "gz"), None, None),
            P(("gx", "gy", "gz"), None, None),
            P(("gx", "gy", "gz")),
            P(("gx", "gy"), "gz"),
            P(("gy", "gx"), "gz"),
            P("gy", ("gx", "gz")),
        ),
        out_specs=(
            P("gy", ("gx", "gz")),
            P(("gy", "gx"), "gz"),
            P(("gx", "gy"), "gz"),
            P(("gx", "gy"), "gz"),
            P(("gx", "gy"), "gz"),
        ),
        check_vma=False,
    )
```

```python
import math

import jax
import jax.numpy as jnp
from jax import lax
from jax.sharding import PartitionSpec as P

D = 12288


BETA_ONE = 0.9
BETA_TWO = 0.95
LEARN_RATE = 0.01
WEIGHT_DECAY = 0.1
EPSILON = 1e-08
BIAS_ONE = 0.9999734386011125
BIAS_TWO = 0.994079470779666
DITHER_SCALE = 0.25


def dither(seeds, position):
    mixing = seeds + position * 1640531527
    mixing = mixing ^ mixing >> 15 & 131071
    mixing = mixing * 739982445
    mixing = mixing ^ mixing >> 12 & 1048575
    mixing = mixing * 695872825
    mixing = mixing ^ mixing >> 15 & 131071
    return (mixing & 65535).astype(jnp.float32) / 65536.0 - 0.5


def body(flat_weight, flat_first, flat_second, tile_map, tile_seeds, tokens, grad_out):
    size_gx = lax.axis_size("gx")
    size_gy = lax.axis_size("gy")
    size_gz = lax.axis_size("gz")
    group_size = size_gx * size_gz
    tiles_own = flat_weight.shape[0]
    tile_side = flat_weight.shape[1]
    row_tiles = tile_seeds.shape[0]
    col_tiles = tile_seeds.shape[1]
    capacity = max(2, (2 * tiles_own + group_size - 1) // group_size - 1)
    total_slots = group_size * capacity
    across = col_tiles * size_gz
    row_block = tile_map // across
    col_block = tile_map % across
    target = row_block // row_tiles // size_gy * size_gz + col_block // col_tiles
    local_tile = row_block % row_tiles * col_tiles + col_block % col_tiles
    ordinal = jnp.arange(tiles_own, dtype=jnp.int32)
    same_owner = (target[:, None] == target[None, :]) & (ordinal[None, :] < ordinal[:, None])
    ranking = jnp.sum(same_owner.astype(jnp.int32), axis=1)
    position = target * capacity + ranking
    slot_ids = jnp.arange(total_slots, dtype=jnp.int32)
    matches = (position[None, :] == slot_ids[:, None]).astype(jnp.int32)
    source = jnp.sum(matches * ordinal[None, :], axis=1)
    filled = jnp.sum(matches, axis=1).astype(jnp.float32)[:, None, None]
    labels = jnp.sum(matches * (local_tile[None, :] + 1), axis=1)
    grid_shape = (group_size, capacity, tile_side, tile_side)
    send_weight = (jnp.take(flat_weight, source, axis=0) * filled).astype(jnp.bfloat16)
    got_labels = lax.all_to_all(
        labels.reshape(group_size, capacity), ("gx", "gz"), split_axis=0, concat_axis=0, tiled=True
    )
    got_weight = lax.all_to_all(
        send_weight.reshape(grid_shape), ("gx", "gz"), split_axis=0, concat_axis=0, tiled=True
    )
    token_band = lax.all_gather(tokens, "gx", axis=0, tiled=True)
    grad_band = lax.all_gather(grad_out.T, "gz", axis=0, tiled=True)
    got_weight, token_band, grad_band = lax.optimization_barrier((got_weight, token_band, grad_band))
    got_weight = got_weight.astype(jnp.float32)
    got_labels = got_labels.reshape(total_slots)
    wanted = jnp.arange(1, tiles_own + 1, dtype=jnp.int32)
    hits = (got_labels[None, :] == wanted[:, None]).astype(jnp.int32)
    picked = jnp.sum(hits * slot_ids[None, :], axis=1)

    def place(received):
        flat_tiles = jnp.take(received.reshape(total_slots, tile_side, tile_side), picked, axis=0)
        tile_grid = flat_tiles.reshape(row_tiles, col_tiles, tile_side, tile_side)
        return tile_grid.transpose(0, 2, 1, 3).reshape(row_tiles * tile_side, col_tiles * tile_side)

    weight = place(got_weight)
    weight_low = weight.astype(jnp.bfloat16)
    send_moments = jnp.stack(
        [jnp.take(flat_first, source, axis=0) * filled, jnp.take(flat_second, source, axis=0) * filled],
        axis=1,
    ).astype(jnp.bfloat16)
    send_moments, weight_low = lax.optimization_barrier((send_moments, weight_low))
    got_moments = lax.all_to_all(
        send_moments.reshape(group_size, capacity, 2, tile_side, tile_side),
        ("gx", "gz"),
        split_axis=0,
        concat_axis=0,
        tiled=True,
    )
    weight_band = lax.all_gather(weight_low, "gy", axis=0, tiled=True)
    got_moments, weight_band = lax.optimization_barrier((got_moments, weight_band))
    got_moments = got_moments.astype(jnp.float32).reshape(total_slots, 2, tile_side, tile_side)
    first_moment = place(got_moments[:, 0])
    second_moment = place(got_moments[:, 1])
    factor = 1.0 / math.sqrt(D)
    partial_out = factor * jnp.dot(token_band, weight_band.T, preferred_element_type=jnp.float32)
    outputs = lax.psum_scatter(
        partial_out.astype(jnp.bfloat16), "gz", scatter_dimension=1, tiled=True
    )
    input_part = (
        factor
        * lax.dot_general(
            grad_band, weight_band, (((0,), (0,)), ((), ())), preferred_element_type=jnp.float32
        )
    ).astype(jnp.bfloat16)
    input_parts = lax.all_to_all(
        input_part.reshape(size_gx, input_part.shape[0] // size_gx, input_part.shape[1]),
        "gx",
        split_axis=0,
        concat_axis=0,
        tiled=True,
    )
    input_grad = jnp.sum(input_parts.astype(jnp.float32), axis=0).astype(jnp.bfloat16)
    gradient = lax.psum_scatter(
        (factor * jnp.dot(grad_band, token_band, preferred_element_type=jnp.float32)).astype(
            jnp.bfloat16
        ),
        "gy",
        scatter_dimension=0,
        tiled=True,
    ).astype(jnp.float32)
    first_new = BETA_ONE * first_moment + (1.0 - BETA_ONE) * gradient
    second_new = BETA_TWO * second_moment + (1.0 - BETA_TWO) * gradient * gradient
    direction = (
        first_new / BIAS_ONE / (jnp.sqrt(second_new / BIAS_TWO) + EPSILON) + WEIGHT_DECAY * weight
    )
    moved = weight - LEARN_RATE * direction
    block_shape = weight.shape
    row_ids = lax.broadcasted_iota(jnp.int32, block_shape, 0)
    col_ids = lax.broadcasted_iota(jnp.int32, block_shape, 1)
    seed_full = jnp.repeat(jnp.repeat(tile_seeds, tile_side, axis=0), tile_side, axis=1)
    noise = dither(seed_full, row_ids % tile_side * tile_side + col_ids % tile_side)
    weight_new = moved + jnp.abs(moved) * DITHER_SCALE * noise
    return (outputs, input_grad, weight_new, first_new, second_new)


def solution(mesh):
    return jax.shard_map(
        body,
        mesh=mesh,
        in_specs=(
            P(("gx", "gy", "gz"), None, None),
            P(("gx", "gy", "gz"), None, None),
            P(("gx", "gy", "gz"), None, None),
            P(("gx", "gy", "gz")),
            P(("gx", "gy"), "gz"),
            P(("gy", "gx"), "gz"),
            P("gy", ("gx", "gz")),
        ),
        out_specs=(
            P("gy", ("gx", "gz")),
            P(("gy", "gx"), "gz"),
            P(("gx", "gy"), "gz"),
            P(("gx", "gy"), "gz"),
            P(("gx", "gy"), "gz"),
        ),
        check_vma=False,
    )
```

```python
import math

import jax
import jax.numpy as jnp
from jax import lax
from jax.sharding import PartitionSpec as P

D = 12288


BETA_ONE = 0.9
BETA_TWO = 0.95
LEARN_RATE = 0.01
WEIGHT_DECAY = 0.1
EPSILON = 1e-08
BIAS_ONE = 0.9999734386011125
BIAS_TWO = 0.994079470779666
DITHER_SCALE = 0.25


def dither(seeds, position):
    mixing = seeds + position * 1640531527
    mixing = mixing ^ mixing >> 15 & 131071
    mixing = mixing * 739982445
    mixing = mixing ^ mixing >> 12 & 1048575
    mixing = mixing * 695872825
    mixing = mixing ^ mixing >> 15 & 131071
    return (mixing & 65535).astype(jnp.float32) / 65536.0 - 0.5


def body(flat_weight, flat_first, flat_second, tile_map, tile_seeds, tokens, grad_out):
    size_gx = lax.axis_size("gx")
    size_gy = lax.axis_size("gy")
    size_gz = lax.axis_size("gz")
    group_size = size_gx * size_gz
    tiles_own = flat_weight.shape[0]
    tile_side = flat_weight.shape[1]
    row_tiles = tile_seeds.shape[0]
    col_tiles = tile_seeds.shape[1]
    capacity = max(2, (2 * tiles_own + group_size - 1) // group_size - 1)
    total_slots = group_size * capacity
    across = col_tiles * size_gz
    row_block = tile_map // across
    col_block = tile_map % across
    target = row_block // row_tiles // size_gy * size_gz + col_block // col_tiles
    local_tile = row_block % row_tiles * col_tiles + col_block % col_tiles
    ordinal = jnp.arange(tiles_own, dtype=jnp.int32)
    same_owner = (target[:, None] == target[None, :]) & (ordinal[None, :] < ordinal[:, None])
    ranking = jnp.sum(same_owner.astype(jnp.int32), axis=1)
    position = target * capacity + ranking
    slot_ids = jnp.arange(total_slots, dtype=jnp.int32)
    matches = (position[None, :] == slot_ids[:, None]).astype(jnp.int32)
    source = jnp.sum(matches * ordinal[None, :], axis=1)
    labels = jnp.sum(matches * (local_tile[None, :] + 1), axis=1)
    grid_shape = (group_size, capacity, tile_side, tile_side)

    def route(flat):
        send = jnp.take(flat, source, axis=0).astype(jnp.bfloat16).reshape(grid_shape)
        return lax.all_to_all(send, ("gx", "gz"), split_axis=0, concat_axis=0, tiled=True)

    got_labels = lax.all_to_all(
        labels.reshape(group_size, capacity), ("gx", "gz"), split_axis=0, concat_axis=0, tiled=True
    )
    got_weight = route(flat_weight)
    token_band = lax.all_gather(tokens, "gx", axis=0, tiled=True)
    got_weight, token_band = lax.optimization_barrier((got_weight, token_band))
    got_labels = got_labels.reshape(total_slots)
    wanted = jnp.arange(1, tiles_own + 1, dtype=jnp.int32)
    hits = (got_labels[None, :] == wanted[:, None]).astype(jnp.int32)
    picked = jnp.sum(hits * slot_ids[None, :], axis=1)

    def place(received):
        flat_tiles = jnp.take(received.reshape(total_slots, tile_side, tile_side), picked, axis=0)
        tile_grid = flat_tiles.reshape(row_tiles, col_tiles, tile_side, tile_side)
        return tile_grid.transpose(0, 2, 1, 3).reshape(row_tiles * tile_side, col_tiles * tile_side)

    weight_low = place(got_weight)
    weight = weight_low.astype(jnp.float32)
    flat_first, flat_second, grad_out, weight_low = lax.optimization_barrier(
        (flat_first, flat_second, grad_out, weight_low)
    )
    weight_band = lax.all_gather(weight_low, "gy", axis=0, tiled=True)
    grad_band = lax.all_gather(grad_out.T, "gz", axis=0, tiled=True)
    got_first = route(flat_first)
    got_second = route(flat_second)
    got_first, got_second, weight_band = lax.optimization_barrier((got_first, got_second, weight_band))
    first_moment = place(got_first).astype(jnp.float32)
    second_moment = place(got_second).astype(jnp.float32)
    factor = 1.0 / math.sqrt(D)
    partial_out = factor * jnp.dot(token_band, weight_band.T, preferred_element_type=jnp.float32)
    outputs = lax.psum_scatter(
        partial_out.astype(jnp.bfloat16), "gz", scatter_dimension=1, tiled=True
    )
    input_part = (
        factor
        * lax.dot_general(
            grad_band, weight_band, (((0,), (0,)), ((), ())), preferred_element_type=jnp.float32
        )
    ).astype(jnp.bfloat16)
    input_parts = lax.all_to_all(
        input_part.reshape(size_gx, input_part.shape[0] // size_gx, input_part.shape[1]),
        "gx",
        split_axis=0,
        concat_axis=0,
        tiled=True,
    )
    input_grad = jnp.sum(input_parts.astype(jnp.float32), axis=0).astype(jnp.bfloat16)
    gradient = lax.psum_scatter(
        (factor * jnp.dot(grad_band, token_band, preferred_element_type=jnp.float32)).astype(
            jnp.bfloat16
        ),
        "gy",
        scatter_dimension=0,
        tiled=True,
    ).astype(jnp.float32)
    first_new = BETA_ONE * first_moment + (1.0 - BETA_ONE) * gradient
    second_new = BETA_TWO * second_moment + (1.0 - BETA_TWO) * gradient * gradient
    direction = (
        first_new / BIAS_ONE / (jnp.sqrt(second_new / BIAS_TWO) + EPSILON) + WEIGHT_DECAY * weight
    )
    moved = weight - LEARN_RATE * direction
    block_shape = weight.shape
    row_ids = lax.broadcasted_iota(jnp.int32, block_shape, 0)
    col_ids = lax.broadcasted_iota(jnp.int32, block_shape, 1)
    seed_full = jnp.repeat(jnp.repeat(tile_seeds, tile_side, axis=0), tile_side, axis=1)
    noise = dither(seed_full, row_ids % tile_side * tile_side + col_ids % tile_side)
    weight_new = moved + jnp.abs(moved) * DITHER_SCALE * noise
    return (outputs, input_grad, weight_new, first_new, second_new)


def solution(mesh):
    return jax.shard_map(
        body,
        mesh=mesh,
        in_specs=(
            P(("gx", "gy", "gz"), None, None),
            P(("gx", "gy", "gz"), None, None),
            P(("gx", "gy", "gz"), None, None),
            P(("gx", "gy", "gz")),
            P(("gx", "gy"), "gz"),
            P(("gy", "gx"), "gz"),
            P("gy", ("gx", "gz")),
        ),
        out_specs=(
            P("gy", ("gx", "gz")),
            P(("gy", "gx"), "gz"),
            P(("gx", "gy"), "gz"),
            P(("gx", "gy"), "gz"),
            P(("gx", "gy"), "gz"),
        ),
        check_vma=False,
    )
```

```python
import math

import jax
import jax.numpy as jnp
from jax import lax
from jax.sharding import PartitionSpec as P

D = 12288


BETA_ONE = 0.9
BETA_TWO = 0.95
LEARN_RATE = 0.01
WEIGHT_DECAY = 0.1
EPSILON = 1e-08
BIAS_ONE = 0.9999734386011125
BIAS_TWO = 0.994079470779666
DITHER_SCALE = 0.25


def dither(seeds, position):
    mixing = seeds + position * 1640531527
    mixing = mixing ^ mixing >> 15 & 131071
    mixing = mixing * 739982445
    mixing = mixing ^ mixing >> 12 & 1048575
    mixing = mixing * 695872825
    mixing = mixing ^ mixing >> 15 & 131071
    return (mixing & 65535).astype(jnp.float32) / 65536.0 - 0.5


def body(flat_weight, flat_first, flat_second, tile_map, tile_seeds, tokens, grad_out):
    size_gx = lax.axis_size("gx")
    size_gy = lax.axis_size("gy")
    size_gz = lax.axis_size("gz")
    group_size = size_gx * size_gz
    tiles_own = flat_weight.shape[0]
    tile_side = flat_weight.shape[1]
    row_tiles = tile_seeds.shape[0]
    col_tiles = tile_seeds.shape[1]
    capacity = max(2, (2 * tiles_own + group_size - 1) // group_size - 1)
    total_slots = group_size * capacity
    across = col_tiles * size_gz
    row_block = tile_map // across
    col_block = tile_map % across
    target = row_block // row_tiles // size_gy * size_gz + col_block // col_tiles
    local_tile = row_block % row_tiles * col_tiles + col_block % col_tiles
    ordinal = jnp.arange(tiles_own, dtype=jnp.int32)
    same_owner = (target[:, None] == target[None, :]) & (ordinal[None, :] < ordinal[:, None])
    ranking = jnp.sum(same_owner.astype(jnp.int32), axis=1)
    position = target * capacity + ranking
    slot_ids = jnp.arange(total_slots, dtype=jnp.int32)
    matches = (position[None, :] == slot_ids[:, None]).astype(jnp.int32)
    source = jnp.sum(matches * ordinal[None, :], axis=1)
    labels = jnp.sum(matches * (local_tile[None, :] + 1), axis=1)

    def route(flat):
        send = jnp.take(flat, source, axis=0).astype(jnp.bfloat16)
        send = send.reshape(group_size, capacity, *flat.shape[1:])
        return lax.all_to_all(send, ("gx", "gz"), split_axis=0, concat_axis=0, tiled=True)

    got_labels = lax.all_to_all(
        labels.reshape(group_size, capacity), ("gx", "gz"), split_axis=0, concat_axis=0, tiled=True
    )
    got_weight = route(flat_weight)
    token_band = lax.all_gather(tokens, "gx", axis=0, tiled=True)
    got_weight, token_band = lax.optimization_barrier((got_weight, token_band))
    got_labels = got_labels.reshape(total_slots)
    wanted = jnp.arange(1, tiles_own + 1, dtype=jnp.int32)
    hits = (got_labels[None, :] == wanted[:, None]).astype(jnp.int32)
    picked = jnp.sum(hits * slot_ids[None, :], axis=1)

    def place(received):
        flat_tiles = jnp.take(received.reshape(total_slots, tile_side, tile_side), picked, axis=0)
        tile_grid = flat_tiles.reshape(row_tiles, col_tiles, tile_side, tile_side)
        return tile_grid.transpose(0, 2, 1, 3).reshape(row_tiles * tile_side, col_tiles * tile_side)

    weight_low = place(got_weight)
    weight = weight_low.astype(jnp.float32)
    flat_first, flat_second, grad_out, weight_low = lax.optimization_barrier(
        (flat_first, flat_second, grad_out, weight_low)
    )
    weight_band = lax.all_gather(weight_low, "gy", axis=0, tiled=True)
    grad_band = lax.all_gather(grad_out.T, "gz", axis=0, tiled=True)
    got_moments = route(jnp.concatenate([flat_first, flat_second], axis=1))
    got_moments, weight_band = lax.optimization_barrier((got_moments, weight_band))
    got_moments = got_moments.reshape(total_slots, 2 * tile_side, tile_side)
    first_moment = place(got_moments[:, :tile_side]).astype(jnp.float32)
    second_moment = place(got_moments[:, tile_side:]).astype(jnp.float32)
    factor = 1.0 / math.sqrt(D)
    partial_out = factor * jnp.dot(token_band, weight_band.T, preferred_element_type=jnp.float32)
    out_parts = lax.all_to_all(
        partial_out.astype(jnp.bfloat16).reshape(
            partial_out.shape[0], size_gz, partial_out.shape[1] // size_gz
        ),
        "gz",
        split_axis=1,
        concat_axis=1,
        tiled=True,
    )
    outputs = jnp.sum(out_parts.astype(jnp.float32), axis=1).astype(jnp.bfloat16)
    input_part = (
        factor
        * lax.dot_general(
            grad_band, weight_band, (((0,), (0,)), ((), ())), preferred_element_type=jnp.float32
        )
    ).astype(jnp.bfloat16)
    input_parts = lax.all_to_all(
        input_part.reshape(size_gx, input_part.shape[0] // size_gx, input_part.shape[1]),
        "gx",
        split_axis=0,
        concat_axis=0,
        tiled=True,
    )
    input_grad = jnp.sum(input_parts.astype(jnp.float32), axis=0).astype(jnp.bfloat16)
    gradient = lax.psum_scatter(
        (factor * jnp.dot(grad_band, token_band, preferred_element_type=jnp.float32)).astype(
            jnp.bfloat16
        ),
        "gy",
        scatter_dimension=0,
        tiled=True,
    ).astype(jnp.float32)
    first_new = BETA_ONE * first_moment + (1.0 - BETA_ONE) * gradient
    second_new = BETA_TWO * second_moment + (1.0 - BETA_TWO) * gradient * gradient
    direction = (
        first_new / BIAS_ONE / (jnp.sqrt(second_new / BIAS_TWO) + EPSILON) + WEIGHT_DECAY * weight
    )
    moved = weight - LEARN_RATE * direction
    block_shape = weight.shape
    row_ids = lax.broadcasted_iota(jnp.int32, block_shape, 0)
    col_ids = lax.broadcasted_iota(jnp.int32, block_shape, 1)
    seed_full = jnp.repeat(jnp.repeat(tile_seeds, tile_side, axis=0), tile_side, axis=1)
    noise = dither(seed_full, row_ids % tile_side * tile_side + col_ids % tile_side)
    weight_new = moved + jnp.abs(moved) * DITHER_SCALE * noise
    return (outputs, input_grad, weight_new, first_new, second_new)


def solution(mesh):
    return jax.shard_map(
        body,
        mesh=mesh,
        in_specs=(
            P(("gx", "gy", "gz"), None, None),
            P(("gx", "gy", "gz"), None, None),
            P(("gx", "gy", "gz"), None, None),
            P(("gx", "gy", "gz")),
            P(("gx", "gy"), "gz"),
            P(("gy", "gx"), "gz"),
            P("gy", ("gx", "gz")),
        ),
        out_specs=(
            P("gy", ("gx", "gz")),
            P(("gy", "gx"), "gz"),
            P(("gx", "gy"), "gz"),
            P(("gx", "gy"), "gz"),
            P(("gx", "gy"), "gz"),
        ),
        check_vma=False,
    )
```

```python
import math

import jax
import jax.numpy as jnp
from jax import lax
from jax.sharding import PartitionSpec as P

D = 12288


BETA_ONE = 0.9
BETA_TWO = 0.95
LEARN_RATE = 0.01
WEIGHT_DECAY = 0.1
EPSILON = 1e-08
BIAS_ONE = 0.9999734386011125
BIAS_TWO = 0.994079470779666
DITHER_SCALE = 0.25


def dither(seeds, position):
    mixing = seeds + position * 1640531527
    mixing = mixing ^ mixing >> 15 & 131071
    mixing = mixing * 739982445
    mixing = mixing ^ mixing >> 12 & 1048575
    mixing = mixing * 695872825
    mixing = mixing ^ mixing >> 15 & 131071
    return (mixing & 65535).astype(jnp.float32) / 65536.0 - 0.5


def body(flat_weight, flat_first, flat_second, tile_map, tile_seeds, tokens, grad_out):
    size_gx = lax.axis_size("gx")
    size_gy = lax.axis_size("gy")
    size_gz = lax.axis_size("gz")
    group_size = size_gx * size_gz
    tiles_own = flat_weight.shape[0]
    tile_side = flat_weight.shape[1]
    row_tiles = tile_seeds.shape[0]
    col_tiles = tile_seeds.shape[1]
    capacity = max(2, (2 * tiles_own + group_size - 1) // group_size - 1)
    total_slots = group_size * capacity
    across = col_tiles * size_gz
    row_block = tile_map // across
    col_block = tile_map % across
    target = row_block // row_tiles // size_gy * size_gz + col_block // col_tiles
    local_tile = row_block % row_tiles * col_tiles + col_block % col_tiles
    ordinal = jnp.arange(tiles_own, dtype=jnp.int32)
    same_owner = (target[:, None] == target[None, :]) & (ordinal[None, :] < ordinal[:, None])
    ranking = jnp.sum(same_owner.astype(jnp.int32), axis=1)
    position = target * capacity + ranking
    slot_ids = jnp.arange(total_slots, dtype=jnp.int32)
    matches = (position[None, :] == slot_ids[:, None]).astype(jnp.int32)
    source = jnp.sum(matches * ordinal[None, :], axis=1)
    labels = jnp.sum(matches * (local_tile[None, :] + 1), axis=1)

    def route(flat):
        send = jnp.take(flat, source, axis=0).astype(jnp.bfloat16)
        send = send.reshape(group_size, capacity, *flat.shape[1:])
        return lax.all_to_all(send, ("gx", "gz"), split_axis=0, concat_axis=0, tiled=True)

    label_rows = jnp.broadcast_to(
        labels.astype(jnp.bfloat16)[:, None, None], (total_slots, 16, tile_side)
    )
    send_weight = jnp.concatenate(
        [jnp.take(flat_weight, source, axis=0).astype(jnp.bfloat16), label_rows], axis=1
    )
    got_weight = lax.all_to_all(
        send_weight.reshape(group_size, capacity, tile_side + 16, tile_side),
        ("gx", "gz"),
        split_axis=0,
        concat_axis=0,
        tiled=True,
    ).reshape(total_slots, tile_side + 16, tile_side)
    token_band = lax.all_gather(tokens, "gx", axis=0, tiled=True)
    got_weight, token_band = lax.optimization_barrier((got_weight, token_band))
    got_labels = got_weight[:, tile_side, 0].astype(jnp.int32)
    got_weight = got_weight[:, :tile_side]
    got_labels = got_labels.reshape(total_slots)
    wanted = jnp.arange(1, tiles_own + 1, dtype=jnp.int32)
    hits = (got_labels[None, :] == wanted[:, None]).astype(jnp.int32)
    picked = jnp.sum(hits * slot_ids[None, :], axis=1)

    def place(received):
        flat_tiles = jnp.take(received.reshape(total_slots, tile_side, tile_side), picked, axis=0)
        tile_grid = flat_tiles.reshape(row_tiles, col_tiles, tile_side, tile_side)
        return tile_grid.transpose(0, 2, 1, 3).reshape(row_tiles * tile_side, col_tiles * tile_side)

    weight_low = place(got_weight)
    weight = weight_low.astype(jnp.float32)
    flat_first, flat_second, grad_out, weight_low = lax.optimization_barrier(
        (flat_first, flat_second, grad_out, weight_low)
    )
    weight_band = lax.all_gather(weight_low, "gy", axis=0, tiled=True)
    grad_band = lax.all_gather(grad_out.T, "gz", axis=0, tiled=True)
    got_moments = route(jnp.concatenate([flat_first, flat_second], axis=1))
    got_moments, weight_band = lax.optimization_barrier((got_moments, weight_band))
    got_moments = got_moments.reshape(total_slots, 2 * tile_side, tile_side)
    first_moment = place(got_moments[:, :tile_side]).astype(jnp.float32)
    second_moment = place(got_moments[:, tile_side:]).astype(jnp.float32)
    factor = 1.0 / math.sqrt(D)
    partial_out = factor * jnp.dot(token_band, weight_band.T, preferred_element_type=jnp.float32)
    out_parts = lax.all_to_all(
        partial_out.astype(jnp.bfloat16).reshape(
            partial_out.shape[0], size_gz, partial_out.shape[1] // size_gz
        ),
        "gz",
        split_axis=1,
        concat_axis=1,
        tiled=True,
    )
    outputs = jnp.sum(out_parts.astype(jnp.float32), axis=1).astype(jnp.bfloat16)
    input_part = (
        factor
        * lax.dot_general(
            grad_band, weight_band, (((0,), (0,)), ((), ())), preferred_element_type=jnp.float32
        )
    ).astype(jnp.bfloat16)
    input_parts = lax.all_to_all(
        input_part.reshape(size_gx, input_part.shape[0] // size_gx, input_part.shape[1]),
        "gx",
        split_axis=0,
        concat_axis=0,
        tiled=True,
    )
    input_grad = jnp.sum(input_parts.astype(jnp.float32), axis=0).astype(jnp.bfloat16)
    gradient = lax.psum_scatter(
        (factor * jnp.dot(grad_band, token_band, preferred_element_type=jnp.float32)).astype(
            jnp.bfloat16
        ),
        "gy",
        scatter_dimension=0,
        tiled=True,
    ).astype(jnp.float32)
    first_new = BETA_ONE * first_moment + (1.0 - BETA_ONE) * gradient
    second_new = BETA_TWO * second_moment + (1.0 - BETA_TWO) * gradient * gradient
    direction = (
        first_new / BIAS_ONE / (jnp.sqrt(second_new / BIAS_TWO) + EPSILON) + WEIGHT_DECAY * weight
    )
    moved = weight - LEARN_RATE * direction
    block_shape = weight.shape
    row_ids = lax.broadcasted_iota(jnp.int32, block_shape, 0)
    col_ids = lax.broadcasted_iota(jnp.int32, block_shape, 1)
    seed_full = jnp.repeat(jnp.repeat(tile_seeds, tile_side, axis=0), tile_side, axis=1)
    noise = dither(seed_full, row_ids % tile_side * tile_side + col_ids % tile_side)
    weight_new = moved + jnp.abs(moved) * DITHER_SCALE * noise
    return (outputs, input_grad, weight_new, first_new, second_new)


def solution(mesh):
    return jax.shard_map(
        body,
        mesh=mesh,
        in_specs=(
            P(("gx", "gy", "gz"), None, None),
            P(("gx", "gy", "gz"), None, None),
            P(("gx", "gy", "gz"), None, None),
            P(("gx", "gy", "gz")),
            P(("gx", "gy"), "gz"),
            P(("gy", "gx"), "gz"),
            P("gy", ("gx", "gz")),
        ),
        out_specs=(
            P("gy", ("gx", "gz")),
            P(("gy", "gx"), "gz"),
            P(("gx", "gy"), "gz"),
            P(("gx", "gy"), "gz"),
            P(("gx", "gy"), "gz"),
        ),
        check_vma=False,
    )
```

```python
import math

import jax
import jax.numpy as jnp
from jax import lax
from jax.sharding import PartitionSpec as P

D = 12288


BETA_ONE = 0.9
BETA_TWO = 0.95
LEARN_RATE = 0.01
WEIGHT_DECAY = 0.1
EPSILON = 1e-08
BIAS_ONE = 0.9999734386011125
BIAS_TWO = 0.994079470779666
DITHER_SCALE = 0.25


def dither(seeds, position):
    mixing = seeds + position * 1640531527
    mixing = mixing ^ mixing >> 15 & 131071
    mixing = mixing * 739982445
    mixing = mixing ^ mixing >> 12 & 1048575
    mixing = mixing * 695872825
    mixing = mixing ^ mixing >> 15 & 131071
    return (mixing & 65535).astype(jnp.float32) / 65536.0 - 0.5


def body(flat_weight, flat_first, flat_second, tile_map, tile_seeds, tokens, grad_out):
    size_gx = lax.axis_size("gx")
    size_gy = lax.axis_size("gy")
    size_gz = lax.axis_size("gz")
    group_size = size_gx * size_gz
    tiles_own = flat_weight.shape[0]
    tile_side = flat_weight.shape[1]
    row_tiles = tile_seeds.shape[0]
    col_tiles = tile_seeds.shape[1]
    capacity = max(2, (2 * tiles_own + group_size - 1) // group_size - 1)
    total_slots = group_size * capacity
    across = col_tiles * size_gz
    row_block = tile_map // across
    col_block = tile_map % across
    target = row_block // row_tiles // size_gy * size_gz + col_block // col_tiles
    local_tile = row_block % row_tiles * col_tiles + col_block % col_tiles
    ordinal = jnp.arange(tiles_own, dtype=jnp.int32)
    same_owner = (target[:, None] == target[None, :]) & (ordinal[None, :] < ordinal[:, None])
    ranking = jnp.sum(same_owner.astype(jnp.int32), axis=1)
    position = target * capacity + ranking
    slot_ids = jnp.arange(total_slots, dtype=jnp.int32)
    matches = (position[None, :] == slot_ids[:, None]).astype(jnp.int32)
    source = jnp.sum(matches * ordinal[None, :], axis=1)
    labels = jnp.sum(matches * (local_tile[None, :] + 1), axis=1)

    def route(flat):
        send = jnp.take(flat, source, axis=0).astype(jnp.bfloat16)
        send = send.reshape(group_size, capacity, *flat.shape[1:])
        return lax.all_to_all(send, ("gx", "gz"), split_axis=0, concat_axis=0, tiled=True)

    got_labels = lax.all_to_all(
        labels.reshape(group_size, capacity), ("gx", "gz"), split_axis=0, concat_axis=0, tiled=True
    )
    got_weight = route(flat_weight)
    token_band = lax.all_gather(tokens, "gx", axis=0, tiled=True)
    got_weight, token_band = lax.optimization_barrier((got_weight, token_band))
    got_labels = got_labels.reshape(total_slots)
    wanted = jnp.arange(1, tiles_own + 1, dtype=jnp.int32)
    hits = (got_labels[None, :] == wanted[:, None]).astype(jnp.int32)
    picked = jnp.sum(hits * slot_ids[None, :], axis=1)

    def place(received):
        flat_tiles = jnp.take(received.reshape(total_slots, tile_side, tile_side), picked, axis=0)
        tile_grid = flat_tiles.reshape(row_tiles, col_tiles, tile_side, tile_side)
        return tile_grid.transpose(0, 2, 1, 3).reshape(row_tiles * tile_side, col_tiles * tile_side)

    weight_low = place(got_weight)
    weight = weight_low.astype(jnp.float32)
    flat_first, flat_second, grad_out, weight_low = lax.optimization_barrier(
        (flat_first, flat_second, grad_out, weight_low)
    )
    weight_band = lax.all_gather(weight_low, "gy", axis=0, tiled=True)
    grad_band = lax.all_gather(grad_out.T, "gz", axis=0, tiled=True)
    got_moments = route(jnp.concatenate([flat_first, flat_second], axis=1))
    got_moments, weight_band = lax.optimization_barrier((got_moments, weight_band))
    got_moments = got_moments.reshape(total_slots, 2 * tile_side, tile_side)
    first_moment = place(got_moments[:, :tile_side]).astype(jnp.float32)
    second_moment = place(got_moments[:, tile_side:]).astype(jnp.float32)
    factor = 1.0 / math.sqrt(D)
    partial_out = factor * jnp.dot(token_band, weight_band.T, preferred_element_type=jnp.float32)
    out_parts = lax.all_to_all(
        partial_out.astype(jnp.bfloat16).reshape(
            partial_out.shape[0], size_gz, partial_out.shape[1] // size_gz
        ),
        "gz",
        split_axis=1,
        concat_axis=1,
        tiled=True,
    )
    outputs = jnp.sum(out_parts.astype(jnp.float32), axis=1).astype(jnp.bfloat16)
    input_part = (
        factor
        * lax.dot_general(
            grad_band, weight_band, (((0,), (0,)), ((), ())), preferred_element_type=jnp.float32
        )
    ).astype(jnp.bfloat16)
    input_parts = lax.all_to_all(
        input_part.reshape(size_gx, input_part.shape[0] // size_gx, input_part.shape[1]),
        "gx",
        split_axis=0,
        concat_axis=0,
        tiled=True,
    )
    input_grad = jnp.sum(input_parts.astype(jnp.float32), axis=0).astype(jnp.bfloat16)
    gradient = lax.psum_scatter(
        (factor * jnp.dot(grad_band, token_band, preferred_element_type=jnp.float32)).astype(
            jnp.bfloat16
        ),
        "gy",
        scatter_dimension=0,
        tiled=True,
    ).astype(jnp.float32)
    block_shape = weight.shape
    row_ids = lax.broadcasted_iota(jnp.int32, block_shape, 0)
    col_ids = lax.broadcasted_iota(jnp.int32, block_shape, 1)
    seed_full = jnp.repeat(jnp.repeat(tile_seeds, tile_side, axis=0), tile_side, axis=1)
    noise = dither(seed_full, row_ids % tile_side * tile_side + col_ids % tile_side)
    noise, input_grad, first_moment, second_moment, weight = lax.optimization_barrier(
        (noise, input_grad, first_moment, second_moment, weight)
    )
    first_new = BETA_ONE * first_moment + (1.0 - BETA_ONE) * gradient
    second_new = BETA_TWO * second_moment + (1.0 - BETA_TWO) * gradient * gradient
    direction = (
        first_new / BIAS_ONE / (jnp.sqrt(second_new / BIAS_TWO) + EPSILON) + WEIGHT_DECAY * weight
    )
    moved = weight - LEARN_RATE * direction
    weight_new = moved + jnp.abs(moved) * DITHER_SCALE * noise
    return (outputs, input_grad, weight_new, first_new, second_new)


def solution(mesh):
    return jax.shard_map(
        body,
        mesh=mesh,
        in_specs=(
            P(("gx", "gy", "gz"), None, None),
            P(("gx", "gy", "gz"), None, None),
            P(("gx", "gy", "gz"), None, None),
            P(("gx", "gy", "gz")),
            P(("gx", "gy"), "gz"),
            P(("gy", "gx"), "gz"),
            P("gy", ("gx", "gz")),
        ),
        out_specs=(
            P("gy", ("gx", "gz")),
            P(("gy", "gx"), "gz"),
            P(("gx", "gy"), "gz"),
            P(("gx", "gy"), "gz"),
            P(("gx", "gy"), "gz"),
        ),
        check_vma=False,
    )
```

```python
import math

import jax
import jax.numpy as jnp
from jax import lax
from jax.sharding import PartitionSpec as P

D = 12288


BETA_ONE = 0.9
BETA_TWO = 0.95
LEARN_RATE = 0.01
WEIGHT_DECAY = 0.1
EPSILON = 1e-08
BIAS_ONE = 0.9999734386011125
BIAS_TWO = 0.994079470779666
DITHER_SCALE = 0.25


def dither(seeds, position):
    mixing = seeds + position * 1640531527
    mixing = mixing ^ mixing >> 15 & 131071
    mixing = mixing * 739982445
    mixing = mixing ^ mixing >> 12 & 1048575
    mixing = mixing * 695872825
    mixing = mixing ^ mixing >> 15 & 131071
    return (mixing & 65535).astype(jnp.float32) / 65536.0 - 0.5


def body(flat_weight, flat_first, flat_second, tile_map, tile_seeds, tokens, grad_out):
    size_gx = lax.axis_size("gx")
    size_gy = lax.axis_size("gy")
    size_gz = lax.axis_size("gz")
    group_size = size_gx * size_gz
    tiles_own = flat_weight.shape[0]
    tile_side = flat_weight.shape[1]
    row_tiles = tile_seeds.shape[0]
    col_tiles = tile_seeds.shape[1]
    capacity = max(2, (2 * tiles_own + group_size - 1) // group_size - 1)
    total_slots = group_size * capacity
    across = col_tiles * size_gz
    row_block = tile_map // across
    col_block = tile_map % across
    target = row_block // row_tiles // size_gy * size_gz + col_block // col_tiles
    local_tile = row_block % row_tiles * col_tiles + col_block % col_tiles
    ordinal = jnp.arange(tiles_own, dtype=jnp.int32)
    same_owner = (target[:, None] == target[None, :]) & (ordinal[None, :] < ordinal[:, None])
    ranking = jnp.sum(same_owner.astype(jnp.int32), axis=1)
    position = target * capacity + ranking
    slot_ids = jnp.arange(total_slots, dtype=jnp.int32)
    matches = (position[None, :] == slot_ids[:, None]).astype(jnp.int32)
    source = jnp.sum(matches * ordinal[None, :], axis=1)
    labels = jnp.sum(matches * (local_tile[None, :] + 1), axis=1)

    def route(flat):
        send = jnp.take(flat, source, axis=0).astype(jnp.bfloat16)
        send = send.reshape(group_size, capacity, *flat.shape[1:])
        return lax.all_to_all(send, ("gx", "gz"), split_axis=0, concat_axis=0, tiled=True)

    got_labels = lax.all_to_all(
        labels.reshape(group_size, capacity), ("gx", "gz"), split_axis=0, concat_axis=0, tiled=True
    )
    got_weight = route(flat_weight)
    token_band = lax.all_gather(tokens, "gx", axis=0, tiled=True)
    got_weight, token_band = lax.optimization_barrier((got_weight, token_band))
    got_labels = got_labels.reshape(total_slots)
    wanted = jnp.arange(1, tiles_own + 1, dtype=jnp.int32)
    hits = (got_labels[None, :] == wanted[:, None]).astype(jnp.int32)
    picked = jnp.sum(hits * slot_ids[None, :], axis=1)

    def place(received):
        flat_tiles = jnp.take(received.reshape(total_slots, tile_side, tile_side), picked, axis=0)
        tile_grid = flat_tiles.reshape(row_tiles, col_tiles, tile_side, tile_side)
        return tile_grid.transpose(0, 2, 1, 3).reshape(row_tiles * tile_side, col_tiles * tile_side)

    weight_low = place(got_weight)
    weight = weight_low.astype(jnp.float32)
    flat_first, flat_second, weight_low = lax.optimization_barrier(
        (flat_first, flat_second, weight_low)
    )
    weight_band = lax.all_gather(weight_low, "gy", axis=0, tiled=True)
    own_gz = lax.axis_index("gz")
    grad_band = lax.psum(
        jnp.zeros((size_gz,) + grad_out.T.shape, grad_out.dtype).at[own_gz].set(grad_out.T), "gz"
    ).reshape(size_gz * grad_out.shape[1], grad_out.shape[0])
    got_moments = route(jnp.concatenate([flat_first, flat_second], axis=1))
    got_moments, weight_band = lax.optimization_barrier((got_moments, weight_band))
    got_moments = got_moments.reshape(total_slots, 2 * tile_side, tile_side)
    first_moment = place(got_moments[:, :tile_side]).astype(jnp.float32)
    second_moment = place(got_moments[:, tile_side:]).astype(jnp.float32)
    factor = 1.0 / math.sqrt(D)
    partial_out = factor * jnp.dot(token_band, weight_band.T, preferred_element_type=jnp.float32)
    out_parts = lax.all_to_all(
        partial_out.astype(jnp.bfloat16).reshape(
            partial_out.shape[0], size_gz, partial_out.shape[1] // size_gz
        ),
        "gz",
        split_axis=1,
        concat_axis=1,
        tiled=True,
    )
    outputs = jnp.sum(out_parts.astype(jnp.float32), axis=1).astype(jnp.bfloat16)
    input_part = (
        factor
        * lax.dot_general(
            grad_band, weight_band, (((0,), (0,)), ((), ())), preferred_element_type=jnp.float32
        )
    ).astype(jnp.bfloat16)
    input_parts = lax.all_to_all(
        input_part.reshape(size_gx, input_part.shape[0] // size_gx, input_part.shape[1]),
        "gx",
        split_axis=0,
        concat_axis=0,
        tiled=True,
    )
    input_grad = jnp.sum(input_parts.astype(jnp.float32), axis=0).astype(jnp.bfloat16)
    gradient = lax.psum_scatter(
        (factor * jnp.dot(grad_band, token_band, preferred_element_type=jnp.float32)).astype(
            jnp.bfloat16
        ),
        "gy",
        scatter_dimension=0,
        tiled=True,
    ).astype(jnp.float32)
    block_shape = weight.shape
    row_ids = lax.broadcasted_iota(jnp.int32, block_shape, 0)
    col_ids = lax.broadcasted_iota(jnp.int32, block_shape, 1)
    seed_full = jnp.repeat(jnp.repeat(tile_seeds, tile_side, axis=0), tile_side, axis=1)
    noise = dither(seed_full, row_ids % tile_side * tile_side + col_ids % tile_side)
    noise, input_grad, first_moment, second_moment, weight = lax.optimization_barrier(
        (noise, input_grad, first_moment, second_moment, weight)
    )
    first_new = BETA_ONE * first_moment + (1.0 - BETA_ONE) * gradient
    second_new = BETA_TWO * second_moment + (1.0 - BETA_TWO) * gradient * gradient
    direction = (
        first_new / BIAS_ONE / (jnp.sqrt(second_new / BIAS_TWO) + EPSILON) + WEIGHT_DECAY * weight
    )
    moved = weight - LEARN_RATE * direction
    weight_new = moved + jnp.abs(moved) * DITHER_SCALE * noise
    return (outputs, input_grad, weight_new, first_new, second_new)


def solution(mesh):
    return jax.shard_map(
        body,
        mesh=mesh,
        in_specs=(
            P(("gx", "gy", "gz"), None, None),
            P(("gx", "gy", "gz"), None, None),
            P(("gx", "gy", "gz"), None, None),
            P(("gx", "gy", "gz")),
            P(("gx", "gy"), "gz"),
            P(("gy", "gx"), "gz"),
            P("gy", ("gx", "gz")),
        ),
        out_specs=(
            P("gy", ("gx", "gz")),
            P(("gy", "gx"), "gz"),
            P(("gx", "gy"), "gz"),
            P(("gx", "gy"), "gz"),
            P(("gx", "gy"), "gz"),
        ),
        check_vma=False,
    )
```

```python
import math

import jax
import jax.numpy as jnp
from jax import lax
from jax.sharding import PartitionSpec as P

D = 12288


BETA_ONE = 0.9
BETA_TWO = 0.95
LEARN_RATE = 0.01
WEIGHT_DECAY = 0.1
EPSILON = 1e-08
BIAS_ONE = 0.9999734386011125
BIAS_TWO = 0.994079470779666
DITHER_SCALE = 0.25


def dither(seeds, position):
    mixing = seeds + position * 1640531527
    mixing = mixing ^ mixing >> 15 & 131071
    mixing = mixing * 739982445
    mixing = mixing ^ mixing >> 12 & 1048575
    mixing = mixing * 695872825
    mixing = mixing ^ mixing >> 15 & 131071
    return (mixing & 65535).astype(jnp.float32) / 65536.0 - 0.5


def body(flat_weight, flat_first, flat_second, tile_map, tile_seeds, tokens, grad_out):
    size_gx = lax.axis_size("gx")
    size_gy = lax.axis_size("gy")
    size_gz = lax.axis_size("gz")
    group_size = size_gx * size_gz
    tiles_own = flat_weight.shape[0]
    tile_side = flat_weight.shape[1]
    row_tiles = tile_seeds.shape[0]
    col_tiles = tile_seeds.shape[1]
    capacity = max(2, (2 * tiles_own + group_size - 1) // group_size - 1)
    total_slots = group_size * capacity
    across = col_tiles * size_gz
    row_block = tile_map // across
    col_block = tile_map % across
    target = row_block // row_tiles // size_gy * size_gz + col_block // col_tiles
    local_tile = row_block % row_tiles * col_tiles + col_block % col_tiles
    ordinal = jnp.arange(tiles_own, dtype=jnp.int32)
    same_owner = (target[:, None] == target[None, :]) & (ordinal[None, :] < ordinal[:, None])
    ranking = jnp.sum(same_owner.astype(jnp.int32), axis=1)
    position = target * capacity + ranking
    slot_ids = jnp.arange(total_slots, dtype=jnp.int32)
    matches = (position[None, :] == slot_ids[:, None]).astype(jnp.int32)
    source = jnp.sum(matches * ordinal[None, :], axis=1)
    labels = jnp.sum(matches * (local_tile[None, :] + 1), axis=1)

    def exchange(send):
        send = send.reshape(group_size, capacity, *send.shape[1:])
        return lax.all_to_all(send, ("gx", "gz"), split_axis=0, concat_axis=0, tiled=True)

    got_labels = lax.all_to_all(
        labels.reshape(group_size, capacity), ("gx", "gz"), split_axis=0, concat_axis=0, tiled=True
    )
    send_weight = jnp.take(flat_weight, source, axis=0).astype(jnp.bfloat16)
    send_weight, flat_first, flat_second = lax.optimization_barrier(
        (send_weight, flat_first, flat_second)
    )
    got_weight = exchange(send_weight)
    send_moments = jnp.take(
        jnp.concatenate([flat_first, flat_second], axis=1), source, axis=0
    ).astype(jnp.bfloat16)
    token_band = lax.all_gather(tokens, "gx", axis=0, tiled=True)
    got_weight, token_band, send_moments = lax.optimization_barrier(
        (got_weight, token_band, send_moments)
    )
    got_labels = got_labels.reshape(total_slots)
    wanted = jnp.arange(1, tiles_own + 1, dtype=jnp.int32)
    hits = (got_labels[None, :] == wanted[:, None]).astype(jnp.int32)
    picked = jnp.sum(hits * slot_ids[None, :], axis=1)

    def place(received):
        flat_tiles = jnp.take(received.reshape(total_slots, tile_side, tile_side), picked, axis=0)
        tile_grid = flat_tiles.reshape(row_tiles, col_tiles, tile_side, tile_side)
        return tile_grid.transpose(0, 2, 1, 3).reshape(row_tiles * tile_side, col_tiles * tile_side)

    weight_low = place(got_weight)
    weight = weight_low.astype(jnp.float32)
    send_moments, grad_out, weight_low = lax.optimization_barrier(
        (send_moments, grad_out, weight_low)
    )
    weight_band = lax.all_gather(weight_low, "gy", axis=0, tiled=True)
    grad_band = lax.all_gather(grad_out.T, "gz", axis=0, tiled=True)
    got_moments = exchange(send_moments)
    got_moments, weight_band = lax.optimization_barrier((got_moments, weight_band))
    got_moments = got_moments.reshape(total_slots, 2 * tile_side, tile_side)
    first_moment = place(got_moments[:, :tile_side]).astype(jnp.float32)
    second_moment = place(got_moments[:, tile_side:]).astype(jnp.float32)
    factor = 1.0 / math.sqrt(D)
    partial_out = factor * jnp.dot(token_band, weight_band.T, preferred_element_type=jnp.float32)
    out_parts = lax.all_to_all(
        partial_out.astype(jnp.bfloat16).reshape(
            partial_out.shape[0], size_gz, partial_out.shape[1] // size_gz
        ),
        "gz",
        split_axis=1,
        concat_axis=1,
        tiled=True,
    )
    outputs = jnp.sum(out_parts.astype(jnp.float32), axis=1).astype(jnp.bfloat16)
    input_part = (
        factor
        * lax.dot_general(
            grad_band, weight_band, (((0,), (0,)), ((), ())), preferred_element_type=jnp.float32
        )
    ).astype(jnp.bfloat16)
    input_parts = lax.all_to_all(
        input_part.reshape(size_gx, input_part.shape[0] // size_gx, input_part.shape[1]),
        "gx",
        split_axis=0,
        concat_axis=0,
        tiled=True,
    )
    input_grad = jnp.sum(input_parts.astype(jnp.float32), axis=0).astype(jnp.bfloat16)
    gradient = lax.psum_scatter(
        (factor * jnp.dot(grad_band, token_band, preferred_element_type=jnp.float32)).astype(
            jnp.bfloat16
        ),
        "gy",
        scatter_dimension=0,
        tiled=True,
    ).astype(jnp.float32)
    block_shape = weight.shape
    row_ids = lax.broadcasted_iota(jnp.int32, block_shape, 0)
    col_ids = lax.broadcasted_iota(jnp.int32, block_shape, 1)
    seed_full = jnp.repeat(jnp.repeat(tile_seeds, tile_side, axis=0), tile_side, axis=1)
    noise = dither(seed_full, row_ids % tile_side * tile_side + col_ids % tile_side)
    noise, input_grad, first_moment, second_moment, weight = lax.optimization_barrier(
        (noise, input_grad, first_moment, second_moment, weight)
    )
    first_new = BETA_ONE * first_moment + (1.0 - BETA_ONE) * gradient
    second_new = BETA_TWO * second_moment + (1.0 - BETA_TWO) * gradient * gradient
    direction = (
        first_new / BIAS_ONE / (jnp.sqrt(second_new / BIAS_TWO) + EPSILON) + WEIGHT_DECAY * weight
    )
    moved = weight - LEARN_RATE * direction
    weight_new = moved + jnp.abs(moved) * DITHER_SCALE * noise
    return (outputs, input_grad, weight_new, first_new, second_new)


def solution(mesh):
    return jax.shard_map(
        body,
        mesh=mesh,
        in_specs=(
            P(("gx", "gy", "gz"), None, None),
            P(("gx", "gy", "gz"), None, None),
            P(("gx", "gy", "gz"), None, None),
            P(("gx", "gy", "gz")),
            P(("gx", "gy"), "gz"),
            P(("gy", "gx"), "gz"),
            P("gy", ("gx", "gz")),
        ),
        out_specs=(
            P("gy", ("gx", "gz")),
            P(("gy", "gx"), "gz"),
            P(("gx", "gy"), "gz"),
            P(("gx", "gy"), "gz"),
            P(("gx", "gy"), "gz"),
        ),
        check_vma=False,
    )
```

```python
import math

import jax
import jax.numpy as jnp
from jax import lax
from jax.sharding import PartitionSpec as P

D = 12288


BETA_ONE = 0.9
BETA_TWO = 0.95
LEARN_RATE = 0.01
WEIGHT_DECAY = 0.1
EPSILON = 1e-08
BIAS_ONE = 0.9999734386011125
BIAS_TWO = 0.994079470779666
DITHER_SCALE = 0.25


def dither(seeds, position):
    mixing = seeds + position * 1640531527
    mixing = mixing ^ mixing >> 15 & 131071
    mixing = mixing * 739982445
    mixing = mixing ^ mixing >> 12 & 1048575
    mixing = mixing * 695872825
    mixing = mixing ^ mixing >> 15 & 131071
    return (mixing & 65535).astype(jnp.float32) / 65536.0 - 0.5


def body(flat_weight, flat_first, flat_second, tile_map, tile_seeds, tokens, grad_out):
    size_gx = lax.axis_size("gx")
    size_gy = lax.axis_size("gy")
    size_gz = lax.axis_size("gz")
    group_size = size_gx * size_gz
    tiles_own = flat_weight.shape[0]
    tile_side = flat_weight.shape[1]
    row_tiles = tile_seeds.shape[0]
    col_tiles = tile_seeds.shape[1]
    capacity = max(2, (2 * tiles_own + group_size - 1) // group_size - 1)
    total_slots = group_size * capacity
    across = col_tiles * size_gz
    row_block = tile_map // across
    col_block = tile_map % across
    target = row_block // row_tiles // size_gy * size_gz + col_block // col_tiles
    local_tile = row_block % row_tiles * col_tiles + col_block % col_tiles
    ordinal = jnp.arange(tiles_own, dtype=jnp.int32)
    same_owner = (target[:, None] == target[None, :]) & (ordinal[None, :] < ordinal[:, None])
    ranking = jnp.sum(same_owner.astype(jnp.int32), axis=1)
    position = target * capacity + ranking
    slot_ids = jnp.arange(total_slots, dtype=jnp.int32)
    matches = (position[None, :] == slot_ids[:, None]).astype(jnp.int32)
    source = jnp.sum(matches * ordinal[None, :], axis=1)
    labels = jnp.sum(matches * (local_tile[None, :] + 1), axis=1)

    def exchange(send):
        send = send.reshape(group_size, capacity, *send.shape[1:])
        return lax.all_to_all(send, ("gx", "gz"), split_axis=0, concat_axis=0, tiled=True)

    got_labels = lax.all_to_all(
        labels.reshape(group_size, capacity), ("gx", "gz"), split_axis=0, concat_axis=0, tiled=True
    )
    send_weight = jnp.take(flat_weight, source, axis=0).astype(jnp.bfloat16)
    send_weight, flat_first, flat_second = lax.optimization_barrier(
        (send_weight, flat_first, flat_second)
    )
    got_weight = exchange(send_weight)
    send_moments = jnp.take(
        jnp.concatenate([flat_first, flat_second], axis=1), source, axis=0
    ).astype(jnp.bfloat16)
    token_band = lax.all_gather(tokens, "gx", axis=0, tiled=True)
    got_weight, token_band, send_moments = lax.optimization_barrier(
        (got_weight, token_band, send_moments)
    )
    got_labels = got_labels.reshape(total_slots)
    wanted = jnp.arange(1, tiles_own + 1, dtype=jnp.int32)
    hits = (got_labels[None, :] == wanted[:, None]).astype(jnp.int32)
    picked = jnp.sum(hits * slot_ids[None, :], axis=1)

    def place(received):
        flat_tiles = jnp.take(received.reshape(total_slots, tile_side, tile_side), picked, axis=0)
        tile_grid = flat_tiles.reshape(row_tiles, col_tiles, tile_side, tile_side)
        return tile_grid.transpose(0, 2, 1, 3).reshape(row_tiles * tile_side, col_tiles * tile_side)

    weight_low = place(got_weight)
    weight = weight_low.astype(jnp.float32)
    send_moments, grad_out, weight_low = lax.optimization_barrier(
        (send_moments, grad_out, weight_low)
    )
    weight_band = lax.all_gather(weight_low, "gy", axis=0, tiled=True)
    grad_band = lax.all_gather(grad_out.T, "gz", axis=0, tiled=True)
    got_moments = exchange(send_moments)
    got_moments, weight_band = lax.optimization_barrier((got_moments, weight_band))
    got_moments = got_moments.reshape(total_slots, 2 * tile_side, tile_side)
    first_low = place(got_moments[:, :tile_side])
    second_low = place(got_moments[:, tile_side:])
    factor = 1.0 / math.sqrt(D)
    partial_out = factor * jnp.dot(token_band, weight_band.T, preferred_element_type=jnp.float32)
    out_parts = lax.all_to_all(
        partial_out.astype(jnp.bfloat16).reshape(
            partial_out.shape[0], size_gz, partial_out.shape[1] // size_gz
        ),
        "gz",
        split_axis=1,
        concat_axis=1,
        tiled=True,
    )
    outputs = jnp.sum(out_parts.astype(jnp.float32), axis=1).astype(jnp.bfloat16)
    input_part = (
        factor
        * lax.dot_general(
            grad_band, weight_band, (((0,), (0,)), ((), ())), preferred_element_type=jnp.float32
        )
    ).astype(jnp.bfloat16)
    input_parts = lax.all_to_all(
        input_part.reshape(size_gx, input_part.shape[0] // size_gx, input_part.shape[1]),
        "gx",
        split_axis=0,
        concat_axis=0,
        tiled=True,
    )
    input_grad = jnp.sum(input_parts.astype(jnp.float32), axis=0).astype(jnp.bfloat16)
    gradient = lax.psum_scatter(
        (factor * jnp.dot(grad_band, token_band, preferred_element_type=jnp.float32)).astype(
            jnp.bfloat16
        ),
        "gy",
        scatter_dimension=0,
        tiled=True,
    ).astype(jnp.float32)
    block_shape = weight.shape
    row_ids = lax.broadcasted_iota(jnp.int32, block_shape, 0)
    col_ids = lax.broadcasted_iota(jnp.int32, block_shape, 1)
    seed_full = jnp.repeat(jnp.repeat(tile_seeds, tile_side, axis=0), tile_side, axis=1)
    input_grad, first_low, second_low, weight_low = lax.optimization_barrier(
        (input_grad, first_low, second_low, weight_low)
    )
    first_moment = first_low.astype(jnp.float32)
    second_moment = second_low.astype(jnp.float32)
    weight = weight_low.astype(jnp.float32)
    noise = dither(seed_full, row_ids % tile_side * tile_side + col_ids % tile_side)
    first_new = BETA_ONE * first_moment + (1.0 - BETA_ONE) * gradient
    second_new = BETA_TWO * second_moment + (1.0 - BETA_TWO) * gradient * gradient
    direction = (
        first_new / BIAS_ONE / (jnp.sqrt(second_new / BIAS_TWO) + EPSILON) + WEIGHT_DECAY * weight
    )
    moved = weight - LEARN_RATE * direction
    weight_new = moved + jnp.abs(moved) * DITHER_SCALE * noise
    return (outputs, input_grad, weight_new, first_new, second_new)


def solution(mesh):
    return jax.shard_map(
        body,
        mesh=mesh,
        in_specs=(
            P(("gx", "gy", "gz"), None, None),
            P(("gx", "gy", "gz"), None, None),
            P(("gx", "gy", "gz"), None, None),
            P(("gx", "gy", "gz")),
            P(("gx", "gy"), "gz"),
            P(("gy", "gx"), "gz"),
            P("gy", ("gx", "gz")),
        ),
        out_specs=(
            P("gy", ("gx", "gz")),
            P(("gy", "gx"), "gz"),
            P(("gx", "gy"), "gz"),
            P(("gx", "gy"), "gz"),
            P(("gx", "gy"), "gz"),
        ),
        check_vma=False,
    )
```

```python
import math

import jax
import jax.numpy as jnp
from jax import lax
from jax.sharding import PartitionSpec as P

D = 12288


BETA_ONE = 0.9
BETA_TWO = 0.95
LEARN_RATE = 0.01
WEIGHT_DECAY = 0.1
EPSILON = 1e-08
BIAS_ONE = 0.9999734386011125
BIAS_TWO = 0.994079470779666
DITHER_SCALE = 0.25


def dither(seeds, position):
    mixing = seeds + position * 1640531527
    mixing = mixing ^ mixing >> 15 & 131071
    mixing = mixing * 739982445
    mixing = mixing ^ mixing >> 12 & 1048575
    mixing = mixing * 695872825
    mixing = mixing ^ mixing >> 15 & 131071
    return (mixing & 65535).astype(jnp.float32) / 65536.0 - 0.5


def body(flat_weight, flat_first, flat_second, tile_map, tile_seeds, tokens, grad_out):
    size_gx = lax.axis_size("gx")
    size_gy = lax.axis_size("gy")
    size_gz = lax.axis_size("gz")
    group_size = size_gx * size_gz
    tiles_own = flat_weight.shape[0]
    tile_side = flat_weight.shape[1]
    row_tiles = tile_seeds.shape[0]
    col_tiles = tile_seeds.shape[1]
    capacity = max(2, (2 * tiles_own + group_size - 1) // group_size - 1)
    total_slots = group_size * capacity
    across = col_tiles * size_gz
    row_block = tile_map // across
    col_block = tile_map % across
    target = row_block // row_tiles // size_gy * size_gz + col_block // col_tiles
    local_tile = row_block % row_tiles * col_tiles + col_block % col_tiles
    ordinal = jnp.arange(tiles_own, dtype=jnp.int32)
    same_owner = (target[:, None] == target[None, :]) & (ordinal[None, :] < ordinal[:, None])
    ranking = jnp.sum(same_owner.astype(jnp.int32), axis=1)
    position = target * capacity + ranking
    slot_ids = jnp.arange(total_slots, dtype=jnp.int32)
    matches = (position[None, :] == slot_ids[:, None]).astype(jnp.int32)
    source = jnp.sum(matches * ordinal[None, :], axis=1)
    labels = jnp.sum(matches * (local_tile[None, :] + 1), axis=1)

    def exchange(send):
        send = send.reshape(group_size, capacity, *send.shape[1:])
        return lax.all_to_all(send, ("gx", "gz"), split_axis=0, concat_axis=0, tiled=True)

    send_weight = jnp.take(flat_weight, source, axis=0).astype(jnp.bfloat16)
    send_weight, flat_first, flat_second = lax.optimization_barrier(
        (send_weight, flat_first, flat_second)
    )
    got_weight = exchange(send_weight)
    labels, _ = lax.optimization_barrier((labels, send_weight))
    got_labels = lax.all_to_all(
        labels.reshape(group_size, capacity), ("gx", "gz"), split_axis=0, concat_axis=0, tiled=True
    )
    send_moments = jnp.take(
        jnp.concatenate([flat_first, flat_second], axis=1), source, axis=0
    ).astype(jnp.bfloat16)
    token_band = lax.all_gather(tokens, "gx", axis=0, tiled=True)
    got_weight, token_band, send_moments = lax.optimization_barrier(
        (got_weight, token_band, send_moments)
    )
    got_labels = got_labels.reshape(total_slots)
    wanted = jnp.arange(1, tiles_own + 1, dtype=jnp.int32)
    hits = (got_labels[None, :] == wanted[:, None]).astype(jnp.int32)
    picked = jnp.sum(hits * slot_ids[None, :], axis=1)

    def place(received):
        flat_tiles = jnp.take(received.reshape(total_slots, tile_side, tile_side), picked, axis=0)
        tile_grid = flat_tiles.reshape(row_tiles, col_tiles, tile_side, tile_side)
        return tile_grid.transpose(0, 2, 1, 3).reshape(row_tiles * tile_side, col_tiles * tile_side)

    weight_low = place(got_weight)
    weight = weight_low.astype(jnp.float32)
    send_moments, grad_out, weight_low = lax.optimization_barrier(
        (send_moments, grad_out, weight_low)
    )
    weight_band = lax.all_gather(weight_low, "gy", axis=0, tiled=True)
    grad_band = lax.all_gather(grad_out.T, "gz", axis=0, tiled=True)
    got_moments = exchange(send_moments)
    got_moments, weight_band = lax.optimization_barrier((got_moments, weight_band))
    got_moments = got_moments.reshape(total_slots, 2 * tile_side, tile_side)
    first_low = place(got_moments[:, :tile_side])
    second_low = place(got_moments[:, tile_side:])
    factor = 1.0 / math.sqrt(D)
    partial_out = factor * jnp.dot(token_band, weight_band.T, preferred_element_type=jnp.float32)
    out_parts = lax.all_to_all(
        partial_out.astype(jnp.bfloat16).reshape(
            partial_out.shape[0], size_gz, partial_out.shape[1] // size_gz
        ),
        "gz",
        split_axis=1,
        concat_axis=1,
        tiled=True,
    )
    outputs = jnp.sum(out_parts.astype(jnp.float32), axis=1).astype(jnp.bfloat16)
    input_part = (
        factor
        * lax.dot_general(
            grad_band, weight_band, (((0,), (0,)), ((), ())), preferred_element_type=jnp.float32
        )
    ).astype(jnp.bfloat16)
    input_parts = lax.all_to_all(
        input_part.reshape(size_gx, input_part.shape[0] // size_gx, input_part.shape[1]),
        "gx",
        split_axis=0,
        concat_axis=0,
        tiled=True,
    )
    input_grad = jnp.sum(input_parts.astype(jnp.float32), axis=0).astype(jnp.bfloat16)
    gradient = lax.psum_scatter(
        (factor * jnp.dot(grad_band, token_band, preferred_element_type=jnp.float32)).astype(
            jnp.bfloat16
        ),
        "gy",
        scatter_dimension=0,
        tiled=True,
    ).astype(jnp.float32)
    block_shape = weight.shape
    row_ids = lax.broadcasted_iota(jnp.int32, block_shape, 0)
    col_ids = lax.broadcasted_iota(jnp.int32, block_shape, 1)
    seed_full = jnp.repeat(jnp.repeat(tile_seeds, tile_side, axis=0), tile_side, axis=1)
    input_grad, first_low, second_low, weight_low = lax.optimization_barrier(
        (input_grad, first_low, second_low, weight_low)
    )
    first_moment = first_low.astype(jnp.float32)
    second_moment = second_low.astype(jnp.float32)
    weight = weight_low.astype(jnp.float32)
    noise = dither(seed_full, row_ids % tile_side * tile_side + col_ids % tile_side)
    first_new = BETA_ONE * first_moment + (1.0 - BETA_ONE) * gradient
    second_new = BETA_TWO * second_moment + (1.0 - BETA_TWO) * gradient * gradient
    direction = (
        first_new / BIAS_ONE / (jnp.sqrt(second_new / BIAS_TWO) + EPSILON) + WEIGHT_DECAY * weight
    )
    moved = weight - LEARN_RATE * direction
    weight_new = moved + jnp.abs(moved) * DITHER_SCALE * noise
    return (outputs, input_grad, weight_new, first_new, second_new)


def solution(mesh):
    return jax.shard_map(
        body,
        mesh=mesh,
        in_specs=(
            P(("gx", "gy", "gz"), None, None),
            P(("gx", "gy", "gz"), None, None),
            P(("gx", "gy", "gz"), None, None),
            P(("gx", "gy", "gz")),
            P(("gx", "gy"), "gz"),
            P(("gy", "gx"), "gz"),
            P("gy", ("gx", "gz")),
        ),
        out_specs=(
            P("gy", ("gx", "gz")),
            P(("gy", "gx"), "gz"),
            P(("gx", "gy"), "gz"),
            P(("gx", "gy"), "gz"),
            P(("gx", "gy"), "gz"),
        ),
        check_vma=False,
    )
```
